256 devices in a mesh: node: 32 (over y, x, z_lo), shot: 8 (over z_hi, core).
Axes of the slice: x: 4, y: 4, z: 8 (z_hi: 4, z_lo: 2; z = z_hi * 2 + z_lo), core: 2. Of those that a mesh axis runs over, the one named last changes fastest.
Arguments:
- spectra: bfloat16 [64, 2, 1024, 4096], P(None, None, 'shot', 'node'), may hold values from -6 to 6
- source_block: int32 [6], replicated, may hold values from 0 to 127
- taper_window: int32 [6, 1024], replicated, may hold values from 0 to 7
Outputs:
- virtual_gathers: bfloat16 [6, 64, 2, 32, 4096], P(None, 'shot', None, None, 'node')
The draws below stay inside these ranges and needn't reach their ends.
All inputs are finite; a program needn't handle non-finite values.
Results may differ from the reference program's by a relative error of at most 0.0047.
Values may be sent and summed in bfloat16 or wider, within the bound.
No kernel may reach another device: no remote copies, remote signals or barrier semaphores. Data moves between devices by JAX's collectives and lax.ppermute only.
A program may use at most 128 MiB of HBM per device.

```python
import jax
import jax.numpy as jnp
from jax import lax

F = 64
SB = 32
ROUNDS = 6
WINDOWS = 8
NODES = 4096
SHOTS = 1024


def touch_ends(entries, rng, smallest, top_value):
    extent = entries.shape
    place = [jax.random.randint(jax.random.fold_in(rng, axis), (), 0, extent[axis]) for axis in range(len(extent))]
    entries = entries.at[tuple(place)].set(smallest)
    longest = extent.index(max(extent))
    place[longest] = (place[longest] + 1) % extent[longest]
    return entries.at[tuple(place)].set(top_value)


def level_of(stream_key, shape, cuts, least, top_value):
    loudness, own = 1.0, jax.random.fold_in(stream_key, 6)
    for axis_at, parts in cuts:
        draws = jnp.exp(jax.random.uniform(jax.random.fold_in(own, axis_at), (parts,), jnp.float32, least / len(cuts), top_value / len(cuts)))
        loudness = loudness * jnp.repeat(draws, shape[axis_at] // parts).reshape([-1 if axis == axis_at else 1 for axis in range(len(shape))])
    return loudness


def bell_draw(own_key, shape, deviation, bound, shards=(), dtype=jnp.bfloat16):
    factor_of = level_of(own_key, shape, shards, -0.22, 0.18) if shards else 1.0
    array = jax.random.normal(own_key, shape, jnp.float32) * deviation * factor_of
    return jnp.minimum(jnp.maximum(array, -bound), bound).astype(dtype)


def setup_inputs(seed: int = 0) -> dict:
    splits = jax.random.split(jax.random.key(seed), 4)
    spectra = bell_draw(splits[0], (F, 2, SHOTS, NODES), 1.0, 6.0, ((2, 8), (3, 32)))
    source_block = touch_ends(jax.random.randint(splits[1], (ROUNDS,), 0, NODES // SB), jax.random.fold_in(splits[1], 1), 0, (NODES // SB) - 1).astype(jnp.int32)
    taper_window = touch_ends(jax.random.randint(splits[2], (ROUNDS, SHOTS), 0, WINDOWS), jax.random.fold_in(splits[2], 1), 0, WINDOWS - 1).astype(jnp.int32)
    return {"spectra": spectra, "source_block": source_block, "taper_window": taper_window}


def taper_weights(taper_windows):
    return 0.5 - 0.5 * jnp.cos(jnp.pi * (taper_windows.astype(jnp.float32) + 1.0) / (WINDOWS + 1.0))

def correlate_one(pair):
    tapered_spectra, receiver_nodes = pair
    tap = tapered_spectra.astype(jnp.float32)
    rec = receiver_nodes.astype(jnp.float32)
    high = lax.Precision.HIGHEST
    real = jnp.dot(tap[0].T, rec[0], precision=high) + jnp.dot(tap[1].T, rec[1], precision=high)
    imag = jnp.dot(tap[0].T, rec[1], precision=high) - jnp.dot(tap[1].T, rec[0], precision=high)
    return jnp.stack((real, imag), axis=0)

def reference(spectra, source_block, taper_window):
    shot_weights = taper_weights(taper_window)
    scale = 1.0 / jnp.sqrt(jnp.float32(SHOTS))
    gather_results = []
    for turn in range(ROUNDS):
        offset = (source_block[turn] * SB).astype(jnp.int32)
        block = lax.dynamic_slice_in_dim(spectra, offset, SB, 3)
        tapered_spectra = (block.astype(jnp.float32) * shot_weights[turn][:, None]).astype(jnp.bfloat16)
        summed = lax.map(correlate_one, (tapered_spectra, spectra))
        gather_results.append((summed * scale).astype(jnp.bfloat16))
    return jnp.stack(gather_results, axis=0)
```

```python
import jax
import jax.numpy as jnp
import numpy as np
from jax import lax
from jax.sharding import Mesh, PartitionSpec as P

SB = 32
ROUNDS = 6
WINDOWS = 8
PLANE = ("y", "x")


def taper_weights(taper_windows):
    return 0.5 - 0.5 * jnp.cos(jnp.pi * (taper_windows.astype(jnp.float32) + 1.0) / (WINDOWS + 1.0))


def gather_sources(spectra, source_block):
    node_dev = spectra.shape[3]
    per_device = node_dev // SB
    zl_size = lax.axis_size("zl")
    me = (lax.axis_index("y") * lax.axis_size("x") + lax.axis_index("x")) * zl_size + lax.axis_index("zl")
    pieces = []
    for turn in range(ROUNDS):
        block = source_block[turn]
        piece = lax.dynamic_slice_in_dim(spectra, block % per_device * SB, SB, 3)
        mine = me == block // per_device
        pieces.append(jnp.where(mine, piece, jnp.zeros_like(piece)))
    stacked = jnp.stack(pieces, axis=1)
    part = lax.psum_scatter(stacked, PLANE, scatter_dimension=0, tiled=True)
    other = lax.ppermute(part, "zl", perm=[(0, 1), (1, 0)])
    part = part + other
    return lax.all_gather(part, PLANE, axis=0, tiled=True)


def body(spectra, source_block, taper_window):
    shot_dev = spectra.shape[2]
    shot_groups = lax.axis_size("zh") * lax.axis_size("c")
    shot_count = shot_dev * shot_groups
    scale = 1.0 / jnp.sqrt(jnp.float32(shot_count))
    shot_weights = taper_weights(taper_window)
    shot_index = lax.axis_index("zh") * lax.axis_size("c") + lax.axis_index("c")
    local_weights = lax.dynamic_slice_in_dim(shot_weights, shot_index * shot_dev, shot_dev, 1)

    source = gather_sources(spectra, source_block)
    tapered = (
        source.astype(jnp.float32) * local_weights[None, :, None, :, None]
    ).astype(jnp.bfloat16)
    real_part = tapered[:, :, 0]
    imag_part = tapered[:, :, 1]
    real_row = jnp.stack((real_part, imag_part), axis=2)
    imag_row = jnp.stack((-imag_part, real_part), axis=2)
    operator = jnp.stack((real_row, imag_row), axis=2)
    summed = jnp.einsum(
        "froCks,fCkn->frosn", operator, spectra, preferred_element_type=jnp.float32
    )
    reduced = lax.psum_scatter(summed * scale, ("zh", "c"), scatter_dimension=0, tiled=True)
    return jnp.transpose(reduced, (1, 0, 2, 3, 4)).astype(jnp.bfloat16)


def solution(mesh):
    devices = np.asarray(mesh.devices).reshape(4, 4, 2, 4, 2)
    fine = Mesh(devices, ("y", "x", "zl", "zh", "c"))
    in_specs = (P(None, None, ("zh", "c"), ("y", "x", "zl")), P(), P())
    out_specs = P(None, ("zh", "c"), None, None, ("y", "x", "zl"))
    return jax.shard_map(body, mesh=fine, in_specs=in_specs, out_specs=out_specs, check_vma=False)
```

```python
import jax
import jax.numpy as jnp
import numpy as np
from jax import lax
from jax.sharding import Mesh, PartitionSpec as P

SB = 32
ROUNDS = 6
WINDOWS = 8
PLANE = ("y", "x")


def taper_weights(taper_windows):
    return 0.5 - 0.5 * jnp.cos(jnp.pi * (taper_windows.astype(jnp.float32) + 1.0) / (WINDOWS + 1.0))


def gather_sources(spectra, source_block):
    node_dev = spectra.shape[3]
    per_device = node_dev // SB
    me = (lax.axis_index("y") * lax.axis_size("x") + lax.axis_index("x")) * lax.axis_size("zl") + lax.axis_index("zl")
    owner = source_block // per_device
    first = source_block % per_device * SB
    column = jnp.arange(ROUNDS * SB, dtype=jnp.int32)
    wanted = first[column // SB] + column % SB
    keep = owner[column // SB] == me
    node = jnp.arange(node_dev, dtype=jnp.int32)
    select = ((node[:, None] == wanted[None, :]) & keep[None, :]).astype(spectra.dtype)
    picked = jnp.einsum("fckn,nq->fcqk", spectra, select, preferred_element_type=jnp.float32)
    picked = picked.astype(spectra.dtype)
    part = lax.psum_scatter(picked, PLANE, scatter_dimension=0, tiled=True)
    other = lax.ppermute(part, "zl", perm=[(0, 1), (1, 0)])
    return lax.all_gather(part + other, PLANE, axis=0, tiled=True)


def body(spectra, source_block, taper_window):
    freqs, _, shot_dev, node_dev = spectra.shape
    shot_groups = lax.axis_size("zh") * lax.axis_size("c")
    scale = 1.0 / jnp.sqrt(jnp.float32(shot_dev * shot_groups))
    shot_weights = taper_weights(taper_window)
    shot_index = lax.axis_index("zh") * lax.axis_size("c") + lax.axis_index("c")
    local_weights = lax.dynamic_slice_in_dim(shot_weights, shot_index * shot_dev, shot_dev, 1)
    weight_rows = jnp.repeat(local_weights, SB, axis=0)

    source = gather_sources(spectra, source_block)
    tapered = (source.astype(jnp.float32) * weight_rows[None, None]).astype(jnp.bfloat16)
    real_part = tapered[:, 0]
    imag_part = tapered[:, 1]
    real_row = jnp.concatenate((real_part, imag_part), axis=2)
    imag_row = jnp.concatenate((-imag_part, real_part), axis=2)
    operator = jnp.stack((real_row, imag_row), axis=1)
    receivers = spectra.reshape(freqs, 2 * shot_dev, node_dev)
    summed = jnp.einsum("foqK,fKn->foqn", operator, receivers, preferred_element_type=jnp.float32)
    reduced = lax.psum_scatter(summed * scale, ("zh", "c"), scatter_dimension=0, tiled=True)
    local_f = reduced.shape[0]
    reduced = reduced.reshape(local_f, 2, ROUNDS, SB, node_dev)
    return jnp.transpose(reduced, (2, 0, 1, 3, 4)).astype(jnp.bfloat16)


def solution(mesh):
    devices = np.asarray(mesh.devices).reshape(4, 4, 2, 4, 2)
    fine = Mesh(devices, ("y", "x", "zl", "zh", "c"))
    in_specs = (P(None, None, ("zh", "c"), ("y", "x", "zl")), P(), P())
    out_specs = P(None, ("zh", "c"), None, None, ("y", "x", "zl"))
    return jax.shard_map(body, mesh=fine, in_specs=in_specs, out_specs=out_specs, check_vma=False)
```

```python
import jax
import jax.numpy as jnp
import numpy as np
from jax import lax
from jax.sharding import Mesh, PartitionSpec as P

SB = 32
ROUNDS = 6
WINDOWS = 8
CHUNKS = 2
PLANE = ("y", "x")


def taper_weights(taper_windows):
    return 0.5 - 0.5 * jnp.cos(jnp.pi * (taper_windows.astype(jnp.float32) + 1.0) / (WINDOWS + 1.0))


def pick_sources(spectra, source_block):
    node_dev = spectra.shape[3]
    per_device = node_dev // SB
    me = (lax.axis_index("y") * lax.axis_size("x") + lax.axis_index("x")) * lax.axis_size("zl") + lax.axis_index("zl")
    owner = source_block // per_device
    first = source_block % per_device * SB
    column = jnp.arange(ROUNDS * SB, dtype=jnp.int32)
    wanted = first[column // SB] + column % SB
    keep = owner[column // SB] == me
    node = jnp.arange(node_dev, dtype=jnp.int32)
    select = ((node[:, None] == wanted[None, :]) & keep[None, :]).astype(spectra.dtype)
    select = select.reshape(node_dev, CHUNKS, ROUNDS * SB // CHUNKS)
    picked = jnp.einsum("fckn,nhq->hfcqk", spectra, select, preferred_element_type=jnp.float32)
    return picked.astype(spectra.dtype)


def broadcast(piece, pending=None):
    part = lax.psum_scatter(piece, PLANE, scatter_dimension=0, tiled=True)
    other = lax.ppermute(part, "zl", perm=[(0, 1), (1, 0)])
    part = part + other
    if pending is not None:
        part, pending = lax.optimization_barrier((part, pending))
    return lax.all_gather(part, PLANE, axis=0, tiled=True), pending


def shot_reduce(partial):
    nz = lax.axis_size("zh")
    nc = lax.axis_size("c")
    zh = lax.axis_index("zh")
    c = lax.axis_index("c")
    freqs = partial.shape[0]
    grouped = partial.reshape(nz, nc, freqs // (nz * nc), *partial.shape[1:])
    send = lax.dynamic_index_in_dim(grouped, 1 - c, axis=1, keepdims=False)
    keep = lax.dynamic_index_in_dim(grouped, c, axis=1, keepdims=False)
    mine = keep + lax.ppermute(send, "c", perm=[(0, 1), (1, 0)])
    half = mine.shape[-1] // 2
    forward = mine[..., :half]
    backward = mine[..., half:]
    up = [(j, (j + 1) % nz) for j in range(nz)]
    down = [(j, (j - 1) % nz) for j in range(nz)]
    acc_f = lax.dynamic_index_in_dim(forward, (zh - 1) % nz, axis=0, keepdims=False)
    acc_b = lax.dynamic_index_in_dim(backward, (zh + 1) % nz, axis=0, keepdims=False)
    for step in range(nz - 1):
        got_f = lax.ppermute(acc_f, "zh", perm=up)
        got_b = lax.ppermute(acc_b, "zh", perm=down)
        acc_f = got_f + lax.dynamic_index_in_dim(forward, (zh - 2 - step) % nz, axis=0, keepdims=False)
        acc_b = got_b + lax.dynamic_index_in_dim(backward, (zh + 2 + step) % nz, axis=0, keepdims=False)
    return jnp.concatenate((acc_f, acc_b), axis=-1)


def body(spectra, source_block, taper_window):
    freqs, _, shot_dev, node_dev = spectra.shape
    shot_groups = lax.axis_size("zh") * lax.axis_size("c")
    scale = 1.0 / jnp.sqrt(jnp.float32(shot_dev * shot_groups))
    shot_weights = taper_weights(taper_window)
    shot_index = lax.axis_index("zh") * lax.axis_size("c") + lax.axis_index("c")
    local_weights = lax.dynamic_slice_in_dim(shot_weights, shot_index * shot_dev, shot_dev, 1)
    weight_rows = jnp.repeat(local_weights, SB, axis=0).reshape(CHUNKS, -1, shot_dev)
    receivers = spectra.reshape(freqs, 2 * shot_dev, node_dev)

    picked = pick_sources(spectra, source_block)
    results = []
    summed = None
    for chunk in range(CHUNKS):
        piece = picked[chunk]
        pending = None
        if summed is not None:
            piece, summed = lax.optimization_barrier((piece, summed))
            pending = shot_reduce(summed * scale)
        source, pending = broadcast(piece, pending)
        if pending is not None:
            results.append(pending)
        tapered = (source.astype(jnp.float32) * weight_rows[chunk][None, None]).astype(jnp.bfloat16)
        real_part = tapered[:, 0]
        imag_part = tapered[:, 1]
        real_row = jnp.concatenate((real_part, imag_part), axis=2)
        imag_row = jnp.concatenate((-imag_part, real_part), axis=2)
        operator = jnp.stack((real_row, imag_row), axis=1)
        summed = jnp.einsum("foqK,fKn->foqn", operator, receivers, preferred_element_type=jnp.float32)
    results.append(shot_reduce(summed * scale))
    reduced = jnp.concatenate(results, axis=2)
    local_f = reduced.shape[0]
    reduced = reduced.reshape(local_f, 2, ROUNDS, SB, node_dev)
    return jnp.transpose(reduced, (2, 0, 1, 3, 4)).astype(jnp.bfloat16)


def solution(mesh):
    devices = np.asarray(mesh.devices).reshape(4, 4, 2, 4, 2)
    fine = Mesh(devices, ("y", "x", "zl", "zh", "c"))
    in_specs = (P(None, None, ("zh", "c"), ("y", "x", "zl")), P(), P())
    out_specs = P(None, ("zh", "c"), None, None, ("y", "x", "zl"))
    return jax.shard_map(body, mesh=fine, in_specs=in_specs, out_specs=out_specs, check_vma=False)
```

```python
import jax
import jax.numpy as jnp
import numpy as np
from jax import lax
from jax.sharding import Mesh, PartitionSpec as P

SB = 32
ROUNDS = 6
WINDOWS = 8
PLANE = ("y", "x")
SHOT = ("zh", "c")


def taper_weights(taper_windows):
    return 0.5 - 0.5 * jnp.cos(jnp.pi * (taper_windows.astype(jnp.float32) + 1.0) / (WINDOWS + 1.0))


def pick_sources(receivers, source_block):
    node_dev = receivers.shape[3]
    per_device = node_dev // SB
    me = (lax.axis_index("y") * lax.axis_size("x") + lax.axis_index("x")) * lax.axis_size("zl") + lax.axis_index("zl")
    owner = source_block // per_device
    first = source_block % per_device * SB
    column = jnp.arange(ROUNDS * SB, dtype=jnp.int32)
    wanted = first[column // SB] + column % SB
    keep = owner[column // SB] == me
    node = jnp.arange(node_dev, dtype=jnp.int32)
    select = ((node[:, None] == wanted[None, :]) & keep[None, :]).astype(receivers.dtype)
    picked = jnp.einsum("fckn,nq->cfqk", receivers, select, preferred_element_type=jnp.float32)
    return picked.astype(receivers.dtype)


def broadcast(picked):
    planes = lax.axis_size("y") * lax.axis_size("x")
    shape = picked.shape
    pieces = picked.reshape(planes, *shape[2:])
    got = lax.all_to_all(pieces, PLANE, 0, 0, tiled=True)
    mine = jnp.sum(got, axis=0, keepdims=True)
    mine = mine + lax.ppermute(mine, "zl", perm=[(0, 1), (1, 0)])
    return lax.all_gather(mine, PLANE, axis=0, tiled=True).reshape(shape)


def body(spectra, source_block, taper_window):
    receivers = lax.all_to_all(spectra, SHOT, 0, 2, tiled=True)
    freqs, _, shots, node_dev = receivers.shape
    scale = 1.0 / jnp.sqrt(jnp.float32(shots))
    weight_rows = jnp.repeat(taper_weights(taper_window), SB, axis=0)

    source = broadcast(pick_sources(receivers, source_block))
    tapered = (source.astype(jnp.float32) * weight_rows[None, None]).astype(jnp.bfloat16)
    real_part = tapered[0]
    imag_part = tapered[1]
    real_row = jnp.concatenate((real_part, imag_part), axis=2)
    imag_row = jnp.concatenate((-imag_part, real_part), axis=2)
    operator = jnp.stack((real_row, imag_row), axis=1)
    stacked = receivers.reshape(freqs, 2 * shots, node_dev)
    summed = jnp.einsum("foqK,fKn->foqn", operator, stacked, preferred_element_type=jnp.float32)
    out = (summed * scale).astype(jnp.bfloat16).reshape(freqs, 2, ROUNDS, SB, node_dev)
    return jnp.transpose(out, (2, 0, 1, 3, 4))


def solution(mesh):
    devices = np.asarray(mesh.devices).reshape(4, 4, 2, 4, 2)
    fine = Mesh(devices, ("y", "x", "zl", "zh", "c"))
    in_specs = (P(None, None, SHOT, ("y", "x", "zl")), P(), P())
    out_specs = P(None, SHOT, None, None, ("y", "x", "zl"))
    return jax.shard_map(body, mesh=fine, in_specs=in_specs, out_specs=out_specs, check_vma=False)
```

```python
import jax
import jax.numpy as jnp
import numpy as np
from jax import lax
from jax.sharding import Mesh, PartitionSpec as P

SB = 32
ROUNDS = 6
WINDOWS = 8
HALVES = 2
PLANE = ("y", "x")
SHOT = ("zh", "c")


def taper_weights(taper_windows):
    return 0.5 - 0.5 * jnp.cos(jnp.pi * (taper_windows.astype(jnp.float32) + 1.0) / (WINDOWS + 1.0))


def selection(node_dev, source_block, dtype):
    per_device = node_dev // SB
    me = (lax.axis_index("y") * lax.axis_size("x") + lax.axis_index("x")) * lax.axis_size("zl") + lax.axis_index("zl")
    owner = source_block // per_device
    first = source_block % per_device * SB
    column = jnp.arange(ROUNDS * SB, dtype=jnp.int32)
    wanted = first[column // SB] + column % SB
    keep = owner[column // SB] == me
    node = jnp.arange(node_dev, dtype=jnp.int32)
    return ((node[:, None] == wanted[None, :]) & keep[None, :]).astype(dtype)


def scatter_piece(receivers, select):
    planes = lax.axis_size("y") * lax.axis_size("x")
    picked = jnp.einsum("fckn,nq->cfqk", receivers, select, preferred_element_type=jnp.float32)
    picked = picked.astype(receivers.dtype)
    pieces = picked.reshape(planes, -1, picked.shape[-1])
    got = lax.all_to_all(pieces, PLANE, 0, 0, tiled=True)
    mine = jnp.sum(got, axis=0, keepdims=True)
    return mine + lax.ppermute(mine, "zl", perm=[(0, 1), (1, 0)])


def body(spectra, source_block, taper_window):
    freqs, comps, shot_dev, node_dev = spectra.shape
    groups = lax.axis_size("zh") * lax.axis_size("c")
    select = selection(node_dev, source_block, spectra.dtype)
    split = spectra.reshape(groups, HALVES, freqs // (groups * HALVES), comps, shot_dev, node_dev)
    receivers = []
    sources = []
    previous = None
    for half in range(HALVES):
        part = split[:, half].reshape(-1, comps, shot_dev, node_dev)
        if previous is not None:
            part, previous = lax.optimization_barrier((part, previous))
            sources.append(lax.all_gather(previous, PLANE, axis=0, tiled=True))
        got = lax.all_to_all(part, SHOT, 0, 2, tiled=True)
        receivers.append(got)
        previous = scatter_piece(got, select)
    sources.append(lax.all_gather(previous, PLANE, axis=0, tiled=True))
    receivers = jnp.concatenate(receivers, axis=0)
    local_f, _, shots, _ = receivers.shape
    fh = local_f // HALVES
    source = jnp.stack([s.reshape(comps, fh, ROUNDS * SB, shots) for s in sources], axis=1)
    source = source.reshape(comps, local_f, ROUNDS * SB, shots)

    scale = 1.0 / jnp.sqrt(jnp.float32(shots))
    weight_rows = jnp.repeat(taper_weights(taper_window), SB, axis=0)
    tapered = (source.astype(jnp.float32) * weight_rows[None, None]).astype(jnp.bfloat16)
    real_part = tapered[0]
    imag_part = tapered[1]
    real_row = jnp.concatenate((real_part, imag_part), axis=2)
    imag_row = jnp.concatenate((-imag_part, real_part), axis=2)
    operator = jnp.stack((real_row, imag_row), axis=1)
    stacked = receivers.reshape(local_f, 2 * shots, node_dev)
    summed = jnp.einsum("foqK,fKn->foqn", operator, stacked, preferred_element_type=jnp.float32)
    out = (summed * scale).astype(jnp.bfloat16).reshape(local_f, 2, ROUNDS, SB, node_dev)
    return jnp.transpose(out, (2, 0, 1, 3, 4))


def solution(mesh):
    devices = np.asarray(mesh.devices).reshape(4, 4, 2, 4, 2)
    fine = Mesh(devices, ("y", "x", "zl", "zh", "c"))
    in_specs = (P(None, None, SHOT, ("y", "x", "zl")), P(), P())
    out_specs = P(None, SHOT, None, None, ("y", "x", "zl"))
    return jax.shard_map(body, mesh=fine, in_specs=in_specs, out_specs=out_specs, check_vma=False)
```

```python
import jax
import jax.numpy as jnp
import numpy as np
from jax import lax
from jax.sharding import Mesh, PartitionSpec as P

SB = 32
ROUNDS = 6
WINDOWS = 8
PLANE = ("y", "x")
SHOT = ("zh", "c")


def taper_weights(taper_windows):
    return 0.5 - 0.5 * jnp.cos(jnp.pi * (taper_windows.astype(jnp.float32) + 1.0) / (WINDOWS + 1.0))


def gather_sources(receivers, source_block):
    freqs, comps, shots, node_dev = receivers.shape
    planes = lax.axis_size("y") * lax.axis_size("x")
    zl_size = lax.axis_size("zl")
    zl = lax.axis_index("zl")
    per_device = node_dev // SB
    slices = receivers.reshape(planes, shots, node_dev)
    plane_nodes = lax.all_to_all(slices, PLANE, 0, 0, tiled=True)
    owner = source_block // per_device
    column = jnp.arange(ROUNDS * SB, dtype=jnp.int32)
    owner_q = owner[column // SB]
    wanted = source_block[column // SB] % per_device * SB + column % SB
    keep = owner_q % zl_size == zl
    node = jnp.arange(node_dev, dtype=jnp.int32)
    where = jnp.arange(planes, dtype=jnp.int32)
    select = (
        (where[:, None, None] == (owner_q // zl_size)[None, None, :])
        & (node[None, :, None] == wanted[None, None, :])
        & keep[None, None, :]
    ).astype(receivers.dtype)
    picked = jnp.einsum("jkn,jnq->qk", plane_nodes, select, preferred_element_type=jnp.float32)
    picked = picked.astype(receivers.dtype)[None]
    picked = picked + lax.ppermute(picked, "zl", perm=[(0, 1), (1, 0)])
    gathered = lax.all_gather(picked, PLANE, axis=0, tiled=True)
    return gathered.reshape(freqs, comps, ROUNDS * SB, shots)


def body(spectra, source_block, taper_window):
    receivers = lax.all_to_all(spectra, SHOT, 0, 2, tiled=True)
    freqs, _, shots, node_dev = receivers.shape
    scale = 1.0 / jnp.sqrt(jnp.float32(shots))
    weight_rows = jnp.repeat(taper_weights(taper_window), SB, axis=0)

    source = gather_sources(receivers, source_block)
    tapered = (source.astype(jnp.float32) * weight_rows[None, None]).astype(jnp.bfloat16)
    real_part = tapered[:, 0]
    imag_part = tapered[:, 1]
    real_row = jnp.concatenate((real_part, imag_part), axis=2)
    imag_row = jnp.concatenate((-imag_part, real_part), axis=2)
    operator = jnp.stack((real_row, imag_row), axis=1)
    stacked = receivers.reshape(freqs, 2 * shots, node_dev)
    summed = jnp.einsum("foqK,fKn->foqn", operator, stacked, preferred_element_type=jnp.float32)
    out = (summed * scale).astype(jnp.bfloat16).reshape(freqs, 2, ROUNDS, SB, node_dev)
    return jnp.transpose(out, (2, 0, 1, 3, 4))


def solution(mesh):
    devices = np.asarray(mesh.devices).reshape(4, 4, 2, 4, 2)
    fine = Mesh(devices, ("y", "x", "zl", "zh", "c"))
    in_specs = (P(None, None, SHOT, ("y", "x", "zl")), P(), P())
    out_specs = P(None, SHOT, None, None, ("y", "x", "zl"))
    return jax.shard_map(body, mesh=fine, in_specs=in_specs, out_specs=out_specs, check_vma=False)
```

```python
import jax
import jax.numpy as jnp
import numpy as np
from jax import lax
from jax.sharding import Mesh, PartitionSpec as P

SB = 32
ROUNDS = 6
WINDOWS = 8
PLANE = ("y", "x")
SHOT = ("zh", "c")


def taper_weights(taper_windows):
    return 0.5 - 0.5 * jnp.cos(jnp.pi * (taper_windows.astype(jnp.float32) + 1.0) / (WINDOWS + 1.0))


def gather_sources(spectra, source_block):
    freqs, comps, shot_dev, node_dev = spectra.shape
    groups = lax.axis_size("zh") * lax.axis_size("c")
    planes = lax.axis_size("y") * lax.axis_size("x")
    zl_size = lax.axis_size("zl")
    zl = lax.axis_index("zl")
    per_device = node_dev // SB
    slots = spectra.reshape(groups, planes, shot_dev, node_dev)
    plane_nodes = lax.all_to_all(slots, PLANE, 1, 1, tiled=True)
    owner = source_block // per_device
    column = jnp.arange(ROUNDS * SB, dtype=jnp.int32)
    owner_q = owner[column // SB]
    wanted = source_block[column // SB] % per_device * SB + column % SB
    keep = owner_q % zl_size == zl
    node = jnp.arange(node_dev, dtype=jnp.int32)
    where = jnp.arange(planes, dtype=jnp.int32)
    select = (
        (where[:, None, None] == (owner_q // zl_size)[None, None, :])
        & (node[None, :, None] == wanted[None, None, :])
        & keep[None, None, :]
    ).astype(spectra.dtype)
    picked = jnp.einsum("gjkn,jnq->gqk", plane_nodes, select, preferred_element_type=jnp.float32)
    picked = picked.astype(spectra.dtype)
    picked = picked + lax.ppermute(picked, "zl", perm=[(0, 1), (1, 0)])
    mine = lax.all_to_all(picked, SHOT, 0, 2, tiled=True)
    gathered = lax.all_gather(mine, PLANE, axis=0, tiled=True)
    return gathered.reshape(freqs // groups, comps, ROUNDS * SB, shot_dev * groups)


def body(spectra, source_block, taper_window):
    source = gather_sources(spectra, source_block)
    receivers = lax.all_to_all(spectra, SHOT, 0, 2, tiled=True)
    freqs, _, shots, node_dev = receivers.shape
    scale = 1.0 / jnp.sqrt(jnp.float32(shots))
    weight_rows = jnp.repeat(taper_weights(taper_window), SB, axis=0)

    tapered = (source.astype(jnp.float32) * weight_rows[None, None]).astype(jnp.bfloat16)
    real_part = tapered[:, 0]
    imag_part = tapered[:, 1]
    real_row = jnp.concatenate((real_part, imag_part), axis=2)
    imag_row = jnp.concatenate((-imag_part, real_part), axis=2)
    operator = jnp.stack((real_row, imag_row), axis=1)
    stacked = receivers.reshape(freqs, 2 * shots, node_dev)
    summed = jnp.einsum("foqK,fKn->foqn", operator, stacked, preferred_element_type=jnp.float32)
    out = (summed * scale).astype(jnp.bfloat16).reshape(freqs, 2, ROUNDS, SB, node_dev)
    return jnp.transpose(out, (2, 0, 1, 3, 4))


def solution(mesh):
    devices = np.asarray(mesh.devices).reshape(4, 4, 2, 4, 2)
    fine = Mesh(devices, ("y", "x", "zl", "zh", "c"))
    in_specs = (P(None, None, SHOT, ("y", "x", "zl")), P(), P())
    out_specs = P(None, SHOT, None, None, ("y", "x", "zl"))
    return jax.shard_map(body, mesh=fine, in_specs=in_specs, out_specs=out_specs, check_vma=False)
```

```python
import jax
import jax.numpy as jnp
import numpy as np
from jax import lax
from jax.sharding import Mesh, PartitionSpec as P

SB = 32
ROUNDS = 6
WINDOWS = 8
PLANE = ("y", "x")
SHOT = ("zh", "c")


def taper_weights(taper_windows):
    return 0.5 - 0.5 * jnp.cos(jnp.pi * (taper_windows.astype(jnp.float32) + 1.0) / (WINDOWS + 1.0))


def gather_sources(spectra, source_block):
    freqs, comps, shot_dev, node_dev = spectra.shape
    groups = lax.axis_size("zh") * lax.axis_size("c")
    planes = lax.axis_size("y") * lax.axis_size("x")
    zl_size = lax.axis_size("zl")
    zl = lax.axis_index("zl")
    per_device = node_dev // SB
    slots = spectra.reshape(groups, planes, shot_dev, node_dev)
    plane_nodes = lax.all_to_all(slots, PLANE, 1, 1, tiled=True)
    owner = source_block // per_device
    column = jnp.arange(ROUNDS * SB, dtype=jnp.int32)
    owner_q = owner[column // SB]
    wanted = source_block[column // SB] % per_device * SB + column % SB
    keep = owner_q % zl_size == zl
    node = jnp.arange(node_dev, dtype=jnp.int32)
    where = jnp.arange(planes, dtype=jnp.int32)
    select = (
        (where[:, None, None] == (owner_q // zl_size)[None, None, :])
        & (node[None, :, None] == wanted[None, None, :])
        & keep[None, None, :]
    ).astype(spectra.dtype)
    picked = jnp.einsum("gjkn,jnq->gqk", plane_nodes, select, preferred_element_type=jnp.float32)
    picked = picked.astype(spectra.dtype)
    picked = picked + lax.ppermute(picked, "zl", perm=[(0, 1), (1, 0)])
    mine = lax.all_to_all(picked, SHOT, 0, 2, tiled=True)
    gathered = lax.all_gather(mine, PLANE, axis=0, tiled=True)
    return gathered.reshape(freqs // groups, comps, ROUNDS * SB, shot_dev * groups)


def exchange_shots(spectra):
    freqs, comps, shot_dev, node_dev = spectra.shape
    nz = lax.axis_size("zh")
    nc = lax.axis_size("c")
    groups = nz * nc
    me = lax.axis_index("zh") * nc + lax.axis_index("c")
    chunks = spectra.reshape(groups, freqs // groups, comps, shot_dev, node_dev)
    arrived = [lax.dynamic_index_in_dim(chunks, me, axis=0, keepdims=False)]
    for shift in range(1, groups):
        target = (me + shift) % groups
        pairs = [(a * nc + b, ((a * nc + b + shift) % groups)) for a in range(nz) for b in range(nc)]
        piece = lax.dynamic_index_in_dim(chunks, target, axis=0, keepdims=False)
        arrived.append(lax.ppermute(piece, SHOT, perm=pairs))
    arrived = jnp.stack(arrived, axis=0)
    order = (me - jnp.arange(groups, dtype=jnp.int32)) % groups
    blocks = jnp.take(arrived, order, axis=0)
    return jnp.transpose(blocks, (1, 2, 0, 3, 4)).reshape(freqs // groups, comps, groups * shot_dev, node_dev)


def body(spectra, source_block, taper_window):
    receivers = exchange_shots(spectra)
    source = gather_sources(spectra, source_block)
    freqs, _, shots, node_dev = receivers.shape
    scale = 1.0 / jnp.sqrt(jnp.float32(shots))
    weight_rows = jnp.repeat(taper_weights(taper_window), SB, axis=0)

    tapered = (source.astype(jnp.float32) * weight_rows[None, None]).astype(jnp.bfloat16)
    real_part = tapered[:, 0]
    imag_part = tapered[:, 1]
    real_row = jnp.concatenate((real_part, imag_part), axis=2)
    imag_row = jnp.concatenate((-imag_part, real_part), axis=2)
    operator = jnp.stack((real_row, imag_row), axis=1)
    stacked = receivers.reshape(freqs, 2 * shots, node_dev)
    summed = jnp.einsum("foqK,fKn->foqn", operator, stacked, preferred_element_type=jnp.float32)
    out = (summed * scale).astype(jnp.bfloat16).reshape(freqs, 2, ROUNDS, SB, node_dev)
    return jnp.transpose(out, (2, 0, 1, 3, 4))


def solution(mesh):
    devices = np.asarray(mesh.devices).reshape(4, 4, 2, 4, 2)
    fine = Mesh(devices, ("y", "x", "zl", "zh", "c"))
    in_specs = (P(None, None, SHOT, ("y", "x", "zl")), P(), P())
    out_specs = P(None, SHOT, None, None, ("y", "x", "zl"))
    return jax.shard_map(body, mesh=fine, in_specs=in_specs, out_specs=out_specs, check_vma=False)
```

```python
import jax
import jax.numpy as jnp
import numpy as np
from jax import lax
from jax.sharding import Mesh, PartitionSpec as P

SB = 32
ROUNDS = 6
WINDOWS = 8
PLANE = ("y", "x")
SHOT = ("zh", "c")


def taper_weights(taper_windows):
    return 0.5 - 0.5 * jnp.cos(jnp.pi * (taper_windows.astype(jnp.float32) + 1.0) / (WINDOWS + 1.0))


def gather_sources(spectra, source_block, receivers=None):
    freqs, comps, shot_dev, node_dev = spectra.shape
    groups = lax.axis_size("zh") * lax.axis_size("c")
    planes = lax.axis_size("y") * lax.axis_size("x")
    zl_size = lax.axis_size("zl")
    per_device = node_dev // SB
    me = (lax.axis_index("y") * lax.axis_size("x") + lax.axis_index("x")) * zl_size + lax.axis_index("zl")
    owner = source_block // per_device
    column = jnp.arange(ROUNDS * SB, dtype=jnp.int32)
    wanted = source_block[column // SB] % per_device * SB + column % SB
    keep = owner[column // SB] == me
    node = jnp.arange(node_dev, dtype=jnp.int32)
    select = ((node[:, None] == wanted[None, :]) & keep[None, :]).astype(spectra.dtype)
    by_group = spectra.reshape(groups, freqs // groups, comps, shot_dev, node_dev)
    picked = jnp.einsum("gfckn,nq->fcgqk", by_group, select, preferred_element_type=jnp.float32)
    picked = picked.astype(spectra.dtype).reshape(planes * groups, ROUNDS * SB, shot_dev)
    slot = lax.psum_scatter(picked, PLANE, scatter_dimension=0, tiled=True)
    if receivers is not None:
        slot, receivers = lax.optimization_barrier((slot, receivers))
    both = jnp.broadcast_to(slot[None], (zl_size,) + slot.shape).reshape(zl_size * groups, ROUNDS * SB, shot_dev)
    got = lax.all_to_all(both, ("zl",) + SHOT, 0, 0, tiled=True)
    got = jnp.sum(got.reshape(zl_size, groups, ROUNDS * SB, shot_dev), axis=0)
    mine = jnp.transpose(got, (1, 0, 2)).reshape(1, ROUNDS * SB, groups * shot_dev)
    gathered = lax.all_gather(mine, PLANE, axis=0, tiled=True)
    return gathered.reshape(freqs // groups, comps, ROUNDS * SB, shot_dev * groups), receivers


def body(spectra, source_block, taper_window):
    receivers = lax.all_to_all(spectra, SHOT, 0, 2, tiled=True)
    source, receivers = gather_sources(spectra, source_block, receivers)
    freqs, _, shots, node_dev = receivers.shape
    scale = 1.0 / jnp.sqrt(jnp.float32(shots))
    weight_rows = jnp.repeat(taper_weights(taper_window), SB, axis=0)

    tapered = (source.astype(jnp.float32) * weight_rows[None, None]).astype(jnp.bfloat16)
    real_part = tapered[:, 0]
    imag_part = tapered[:, 1]
    real_row = jnp.concatenate((real_part, imag_part), axis=2)
    imag_row = jnp.concatenate((-imag_part, real_part), axis=2)
    operator = jnp.stack((real_row, imag_row), axis=1)
    stacked = receivers.reshape(freqs, 2 * shots, node_dev)
    summed = jnp.einsum("foqK,fKn->foqn", operator, stacked, preferred_element_type=jnp.float32)
    out = (summed * scale).astype(jnp.bfloat16).reshape(freqs, 2, ROUNDS, SB, node_dev)
    return jnp.transpose(out, (2, 0, 1, 3, 4))


def solution(mesh):
    devices = np.asarray(mesh.devices).reshape(4, 4, 2, 4, 2)
    fine = Mesh(devices, ("y", "x", "zl", "zh", "c"))
    in_specs = (P(None, None, SHOT, ("y", "x", "zl")), P(), P())
    out_specs = P(None, SHOT, None, None, ("y", "x", "zl"))
    return jax.shard_map(body, mesh=fine, in_specs=in_specs, out_specs=out_specs, check_vma=False)
```

```python
import jax
import jax.numpy as jnp
import numpy as np
from jax import lax
from jax.sharding import Mesh, PartitionSpec as P

SB = 32
ROUNDS = 6
WINDOWS = 8
PLANE = ("y", "x")
SHOT = ("zh", "c")


def taper_weights(taper_windows):
    return 0.5 - 0.5 * jnp.cos(jnp.pi * (taper_windows.astype(jnp.float32) + 1.0) / (WINDOWS + 1.0))


def gather_sources(spectra, source_block, receivers=None):
    freqs, comps, shot_dev, node_dev = spectra.shape
    groups = lax.axis_size("zh") * lax.axis_size("c")
    planes = lax.axis_size("y") * lax.axis_size("x")
    zl_size = lax.axis_size("zl")
    per_device = node_dev // SB
    me = (lax.axis_index("y") * lax.axis_size("x") + lax.axis_index("x")) * zl_size + lax.axis_index("zl")
    owner = source_block // per_device
    column = jnp.arange(ROUNDS * SB, dtype=jnp.int32)
    wanted = source_block[column // SB] % per_device * SB + column % SB
    keep = owner[column // SB] == me
    node = jnp.arange(node_dev, dtype=jnp.int32)
    select = ((node[:, None] == wanted[None, :]) & keep[None, :]).astype(spectra.dtype)
    by_group = spectra.reshape(groups, freqs // groups, comps, shot_dev, node_dev)
    picked = jnp.einsum("gfckn,nq->fcgqk", by_group, select, preferred_element_type=jnp.float32)
    picked = picked.astype(spectra.dtype).reshape(planes * groups, ROUNDS * SB, shot_dev)
    slot = lax.psum_scatter(picked, PLANE, scatter_dimension=0, tiled=True)
    if receivers is not None:
        slot, receivers = lax.optimization_barrier((slot, receivers))
    both = jnp.broadcast_to(slot[None], (zl_size,) + slot.shape).reshape(zl_size * groups, ROUNDS * SB, shot_dev)
    got = lax.all_to_all(both, ("zl",) + SHOT, 0, 0, tiled=True)
    got = jnp.sum(got.reshape(zl_size, groups, ROUNDS * SB, shot_dev), axis=0)
    mine = jnp.transpose(got, (1, 0, 2)).reshape(1, ROUNDS * SB, groups * shot_dev)
    return mine, receivers


def exchange(part):
    return lax.all_to_all(part, SHOT, 0, 2, tiled=True)


def body(spectra, source_block, taper_window):
    freqs_all, comps, shot_dev, node_dev = spectra.shape
    groups = lax.axis_size("zh") * lax.axis_size("c")
    split = spectra.reshape(groups, 2, freqs_all // (groups * 2), comps, shot_dev, node_dev)
    first = exchange(split[:, 0].reshape(-1, comps, shot_dev, node_dev))
    mine, first = gather_sources(spectra, source_block, first)
    second_part, mine = lax.optimization_barrier((split[:, 1].reshape(-1, comps, shot_dev, node_dev), mine))
    gathered = lax.all_gather(mine, PLANE, axis=0, tiled=True)
    second = exchange(second_part)
    receivers = jnp.concatenate((first, second), axis=0)
    freqs, _, shots, _ = receivers.shape
    source = gathered.reshape(freqs, comps, ROUNDS * SB, shots)
    scale = 1.0 / jnp.sqrt(jnp.float32(shots))
    weight_rows = jnp.repeat(taper_weights(taper_window), SB, axis=0)

    tapered = (source.astype(jnp.float32) * weight_rows[None, None]).astype(jnp.bfloat16)
    real_part = tapered[:, 0]
    imag_part = tapered[:, 1]
    real_row = jnp.concatenate((real_part, imag_part), axis=2)
    imag_row = jnp.concatenate((-imag_part, real_part), axis=2)
    operator = jnp.stack((real_row, imag_row), axis=1)
    stacked = receivers.reshape(freqs, 2 * shots, node_dev)
    summed = jnp.einsum("foqK,fKn->foqn", operator, stacked, preferred_element_type=jnp.float32)
    out = (summed * scale).astype(jnp.bfloat16).reshape(freqs, 2, ROUNDS, SB, node_dev)
    return jnp.transpose(out, (2, 0, 1, 3, 4))


def solution(mesh):
    devices = np.asarray(mesh.devices).reshape(4, 4, 2, 4, 2)
    fine = Mesh(devices, ("y", "x", "zl", "zh", "c"))
    in_specs = (P(None, None, SHOT, ("y", "x", "zl")), P(), P())
    out_specs = P(None, SHOT, None, None, ("y", "x", "zl"))
    return jax.shard_map(body, mesh=fine, in_specs=in_specs, out_specs=out_specs, check_vma=False)
```

```python
import jax
import jax.numpy as jnp
import numpy as np
from jax import lax
from jax.sharding import Mesh, PartitionSpec as P

SB = 32
ROUNDS = 6
WINDOWS = 8
PLANE = ("y", "x")
SHOT = ("zh", "c")


def taper_weights(taper_windows):
    return 0.5 - 0.5 * jnp.cos(jnp.pi * (taper_windows.astype(jnp.float32) + 1.0) / (WINDOWS + 1.0))


def gather_sources(spectra, source_block, receivers=None):
    freqs, comps, shot_dev, node_dev = spectra.shape
    groups = lax.axis_size("zh") * lax.axis_size("c")
    planes = lax.axis_size("y") * lax.axis_size("x")
    zl_size = lax.axis_size("zl")
    per_device = node_dev // SB
    me = (lax.axis_index("y") * lax.axis_size("x") + lax.axis_index("x")) * zl_size + lax.axis_index("zl")
    block = jnp.repeat(source_block, SB, total_repeat_length=ROUNDS * SB)
    column = jnp.arange(ROUNDS * SB, dtype=jnp.int32)
    wanted = block % per_device * SB + column % SB
    keep = block // per_device == me
    node = jnp.arange(node_dev, dtype=jnp.int32)
    select = ((node[:, None] == wanted[None, :]) & keep[None, :]).astype(spectra.dtype)
    by_group = spectra.reshape(groups, freqs // groups, comps, shot_dev, node_dev)
    picked = jnp.einsum("gfckn,nq->fcgqk", by_group, select, preferred_element_type=jnp.float32)
    picked = picked.astype(spectra.dtype).reshape(planes * groups, ROUNDS * SB, shot_dev)
    slot = lax.psum_scatter(picked, PLANE, scatter_dimension=0, tiled=True)
    if receivers is not None:
        slot, receivers = lax.optimization_barrier((slot, receivers))
    both = jnp.broadcast_to(slot[None], (zl_size,) + slot.shape).reshape(zl_size * groups, ROUNDS * SB, shot_dev)
    got = lax.all_to_all(both, ("zl",) + SHOT, 0, 0, tiled=True)
    got = jnp.sum(got.reshape(zl_size, groups, ROUNDS * SB, shot_dev), axis=0)
    mine = jnp.transpose(got, (1, 0, 2)).reshape(1, ROUNDS * SB, groups * shot_dev)
    return mine, receivers


def exchange(part):
    return lax.all_to_all(part, SHOT, 0, 2, tiled=True)


def body(spectra, source_block, taper_window):
    freqs_all, comps, shot_dev, node_dev = spectra.shape
    groups = lax.axis_size("zh") * lax.axis_size("c")
    split = spectra.reshape(groups, 2, freqs_all // (groups * 2), comps, shot_dev, node_dev)
    first = exchange(split[:, 0].reshape(-1, comps, shot_dev, node_dev))
    mine, first = gather_sources(spectra, source_block, first)
    second_part, mine = lax.optimization_barrier((split[:, 1].reshape(-1, comps, shot_dev, node_dev), mine))
    gathered = lax.all_gather(mine, PLANE, axis=0, tiled=True)
    second = exchange(second_part)
    receivers = jnp.concatenate((first, second), axis=0)
    freqs, _, shots, _ = receivers.shape
    source = gathered.reshape(freqs, comps, ROUNDS * SB, shots)
    scale = 1.0 / jnp.sqrt(jnp.float32(shots))
    weight_rows = jnp.repeat(taper_weights(taper_window), SB, axis=0)

    tapered = (source.astype(jnp.float32) * weight_rows[None, None]).astype(jnp.bfloat16)
    real_part = tapered[:, 0]
    imag_part = tapered[:, 1]
    real_row = jnp.concatenate((real_part, imag_part), axis=2)
    imag_row = jnp.concatenate((-imag_part, real_part), axis=2)
    operator = jnp.stack((real_row, imag_row), axis=1)
    stacked = receivers.reshape(freqs, 2 * shots, node_dev)
    summed = jnp.einsum("foqK,fKn->foqn", operator, stacked, preferred_element_type=jnp.float32)
    out = (summed * scale).astype(jnp.bfloat16).reshape(freqs, 2, ROUNDS, SB, node_dev)
    return jnp.transpose(out, (2, 0, 1, 3, 4))


def solution(mesh):
    devices = np.asarray(mesh.devices).reshape(4, 4, 2, 4, 2)
    fine = Mesh(devices, ("y", "x", "zl", "zh", "c"))
    in_specs = (P(None, None, SHOT, ("y", "x", "zl")), P(), P())
    out_specs = P(None, SHOT, None, None, ("y", "x", "zl"))
    return jax.shard_map(body, mesh=fine, in_specs=in_specs, out_specs=out_specs, check_vma=False)
```

```python
import jax
import jax.numpy as jnp
import numpy as np
from jax import lax
from jax.sharding import Mesh, PartitionSpec as P

SB = 32
ROUNDS = 6
WINDOWS = 8
PLANE = ("y", "x")
SHOT = ("zh", "c")


def taper_weights(taper_windows):
    return 0.5 - 0.5 * jnp.cos(jnp.pi * (taper_windows.astype(jnp.float32) + 1.0) / (WINDOWS + 1.0))


def gather_sources(spectra, source_block, receivers=None):
    freqs, comps, shot_dev, node_dev = spectra.shape
    groups = lax.axis_size("zh") * lax.axis_size("c")
    planes = lax.axis_size("y") * lax.axis_size("x")
    zl_size = lax.axis_size("zl")
    per_device = node_dev // SB
    me = (lax.axis_index("y") * lax.axis_size("x") + lax.axis_index("x")) * zl_size + lax.axis_index("zl")
    block = jnp.repeat(source_block, SB, total_repeat_length=ROUNDS * SB)
    column = jnp.arange(ROUNDS * SB, dtype=jnp.int32)
    wanted = block % per_device * SB + column % SB
    keep = block // per_device == me
    node = jnp.arange(node_dev, dtype=jnp.int32)
    select = ((node[:, None] == wanted[None, :]) & keep[None, :]).astype(spectra.dtype)
    by_group = spectra.reshape(groups, freqs // groups, comps, shot_dev, node_dev)
    picked = jnp.einsum("gfckn,nq->fcgqk", by_group, select, preferred_element_type=jnp.float32)
    picked = picked.astype(spectra.dtype).reshape(planes * groups, ROUNDS * SB, shot_dev)
    slot = lax.psum_scatter(picked, PLANE, scatter_dimension=0, tiled=True)
    if receivers is not None:
        slot, receivers = lax.optimization_barrier((slot, receivers))
    both = jnp.broadcast_to(slot[None], (zl_size,) + slot.shape).reshape(zl_size * groups, ROUNDS * SB, shot_dev)
    got = lax.all_to_all(both, ("zl",) + SHOT, 0, 0, tiled=True)
    got = jnp.sum(got.reshape(zl_size, groups, ROUNDS * SB, shot_dev), axis=0)
    mine = jnp.transpose(got, (1, 0, 2)).reshape(1, ROUNDS * SB, groups * shot_dev)
    return mine, receivers


def exchange(part):
    return lax.all_to_all(part, SHOT, 0, 2, tiled=True)


def body(spectra, source_block, taper_window):
    freqs_all, comps, shot_dev, node_dev = spectra.shape
    groups = lax.axis_size("zh") * lax.axis_size("c")
    split = spectra.reshape(groups, 2, freqs_all // (groups * 2), comps, shot_dev, node_dev)
    first = exchange(split[:, 0].reshape(-1, comps, shot_dev, node_dev))
    mine, first = gather_sources(spectra, source_block, first)
    weight_rows = jnp.repeat(taper_weights(taper_window), SB, axis=0)
    mine = (mine.astype(jnp.float32) * weight_rows[None]).astype(jnp.bfloat16)
    second_part, mine = lax.optimization_barrier((split[:, 1].reshape(-1, comps, shot_dev, node_dev), mine))
    gathered = lax.all_gather(mine, PLANE, axis=0, tiled=True)
    second = exchange(second_part)
    receivers = jnp.concatenate((first, second), axis=0)
    freqs, _, shots, _ = receivers.shape
    tapered = gathered.reshape(freqs, comps, ROUNDS * SB, shots)
    scale = 1.0 / jnp.sqrt(jnp.float32(shots))

    def dot(a, b):
        return jnp.einsum("fqk,fkn->fqn", a, b, preferred_element_type=jnp.float32)

    real_part, imag_part = tapered[:, 0], tapered[:, 1]
    rec_real, rec_imag = receivers[:, 0], receivers[:, 1]
    real = dot(real_part, rec_real) + dot(imag_part, rec_imag)
    imag = dot(real_part, rec_imag) - dot(imag_part, rec_real)
    summed = jnp.stack((real, imag), axis=1)
    out = (summed * scale).astype(jnp.bfloat16).reshape(freqs, 2, ROUNDS, SB, node_dev)
    return jnp.transpose(out, (2, 0, 1, 3, 4))


def solution(mesh):
    devices = np.asarray(mesh.devices).reshape(4, 4, 2, 4, 2)
    fine = Mesh(devices, ("y", "x", "zl", "zh", "c"))
    in_specs = (P(None, None, SHOT, ("y", "x", "zl")), P(), P())
    out_specs = P(None, SHOT, None, None, ("y", "x", "zl"))
    return jax.shard_map(body, mesh=fine, in_specs=in_specs, out_specs=out_specs, check_vma=False)
```

```python
import jax
import jax.numpy as jnp
import numpy as np
from jax import lax
from jax.sharding import Mesh, PartitionSpec as P

SB = 32
ROUNDS = 6
WINDOWS = 8
PLANE = ("y", "x")
SHOT = ("zh", "c")


def taper_weights(taper_windows):
    return 0.5 - 0.5 * jnp.cos(jnp.pi * (taper_windows.astype(jnp.float32) + 1.0) / (WINDOWS + 1.0))


def gather_sources(spectra, source_block, receivers=None):
    freqs, comps, shot_dev, node_dev = spectra.shape
    groups = lax.axis_size("zh") * lax.axis_size("c")
    planes = lax.axis_size("y") * lax.axis_size("x")
    zl_size = lax.axis_size("zl")
    per_device = node_dev // SB
    me = (lax.axis_index("y") * lax.axis_size("x") + lax.axis_index("x")) * zl_size + lax.axis_index("zl")
    block = jnp.repeat(source_block, SB, total_repeat_length=ROUNDS * SB)
    column = jnp.arange(ROUNDS * SB, dtype=jnp.int32)
    wanted = block % per_device * SB + column % SB
    keep = block // per_device == me
    node = jnp.arange(node_dev, dtype=jnp.int32)
    select = ((node[:, None] == wanted[None, :]) & keep[None, :]).astype(spectra.dtype)
    by_slot = jnp.transpose(spectra.reshape(groups, planes, shot_dev, node_dev), (1, 0, 2, 3))
    picked = jnp.einsum("pgkn,nq->pgqk", by_slot, select, preferred_element_type=jnp.float32)
    picked = picked.astype(spectra.dtype).reshape(planes * groups, ROUNDS * SB, shot_dev)
    slot = lax.psum_scatter(picked, PLANE, scatter_dimension=0, tiled=True)
    if receivers is not None:
        slot, receivers = lax.optimization_barrier((slot, receivers))
    both = jnp.broadcast_to(slot[None], (zl_size,) + slot.shape).reshape(zl_size * groups, ROUNDS * SB, shot_dev)
    got = lax.all_to_all(both, ("zl",) + SHOT, 0, 0, tiled=True)
    got = jnp.sum(got.reshape(zl_size, groups, ROUNDS * SB, shot_dev), axis=0)
    mine = jnp.transpose(got, (1, 0, 2)).reshape(1, ROUNDS * SB, groups * shot_dev)
    return mine, receivers


def exchange(part):
    return lax.all_to_all(part, SHOT, 0, 2, tiled=True)


def body(spectra, source_block, taper_window):
    freqs_all, comps, shot_dev, node_dev = spectra.shape
    groups = lax.axis_size("zh") * lax.axis_size("c")
    split = spectra.reshape(groups, 2, freqs_all // (groups * 2), comps, shot_dev, node_dev)
    first = exchange(split[:, 0].reshape(-1, comps, shot_dev, node_dev))
    mine, first = gather_sources(spectra, source_block, first)
    second_part, mine = lax.optimization_barrier((split[:, 1].reshape(-1, comps, shot_dev, node_dev), mine))
    gathered = lax.all_gather(mine, PLANE, axis=0, tiled=True)
    second = exchange(second_part)
    receivers = jnp.concatenate((first, second), axis=0)
    freqs, _, shots, _ = receivers.shape
    source = gathered.reshape(freqs, comps, ROUNDS * SB, shots)
    scale = 1.0 / jnp.sqrt(jnp.float32(shots))
    weight_rows = jnp.repeat(taper_weights(taper_window), SB, axis=0)

    tapered = (source.astype(jnp.float32) * weight_rows[None, None]).astype(jnp.bfloat16)
    real_part = tapered[:, 0]
    imag_part = tapered[:, 1]
    real_row = jnp.concatenate((real_part, imag_part), axis=2)
    imag_row = jnp.concatenate((-imag_part, real_part), axis=2)
    operator = jnp.stack((real_row, imag_row), axis=1)
    stacked = receivers.reshape(freqs, 2 * shots, node_dev)
    summed = jnp.einsum("foqK,fKn->foqn", operator, stacked, preferred_element_type=jnp.float32)
    out = (summed * scale).astype(jnp.bfloat16).reshape(freqs, 2, ROUNDS, SB, node_dev)
    return jnp.transpose(out, (2, 0, 1, 3, 4))


def solution(mesh):
    devices = np.asarray(mesh.devices).reshape(4, 4, 2, 4, 2)
    fine = Mesh(devices, ("y", "x", "zl", "zh", "c"))
    in_specs = (P(None, None, SHOT, ("y", "x", "zl")), P(), P())
    out_specs = P(None, SHOT, None, None, ("y", "x", "zl"))
    return jax.shard_map(body, mesh=fine, in_specs=in_specs, out_specs=out_specs, check_vma=False)
```

```python
import jax
import jax.numpy as jnp
import numpy as np
from jax import lax
from jax.sharding import Mesh, PartitionSpec as P

SB = 32
ROUNDS = 6
WINDOWS = 8
PLANE = ("y", "x")
SHOT = ("zh", "c")


def taper_weights(taper_windows):
    return 0.5 - 0.5 * jnp.cos(jnp.pi * (taper_windows.astype(jnp.float32) + 1.0) / (WINDOWS + 1.0))


def gather_sources(spectra, source_block, receivers=None):
    freqs, comps, shot_dev, node_dev = spectra.shape
    groups = lax.axis_size("zh") * lax.axis_size("c")
    planes = lax.axis_size("y") * lax.axis_size("x")
    zl_size = lax.axis_size("zl")
    per_device = node_dev // SB
    me = (lax.axis_index("y") * lax.axis_size("x") + lax.axis_index("x")) * zl_size + lax.axis_index("zl")
    block = jnp.broadcast_to(source_block[:, None], (ROUNDS, SB)).reshape(ROUNDS * SB)
    column = jnp.arange(ROUNDS * SB, dtype=jnp.int32)
    wanted = block % per_device * SB + column % SB
    keep = block // per_device == me
    node = jnp.arange(node_dev, dtype=jnp.int32)
    select = ((node[:, None] == wanted[None, :]) & keep[None, :]).astype(spectra.dtype)
    by_slot = jnp.transpose(spectra.reshape(groups, planes, shot_dev, node_dev), (1, 0, 2, 3))
    picked = jnp.einsum("pgkn,nq->pgqk", by_slot, select, preferred_element_type=jnp.float32)
    picked = picked.astype(spectra.dtype).reshape(planes * groups, ROUNDS * SB, shot_dev)
    slot = lax.psum_scatter(picked, PLANE, scatter_dimension=0, tiled=True)
    if receivers is not None:
        slot, receivers = lax.optimization_barrier((slot, receivers))
    both = jnp.broadcast_to(slot[None], (zl_size,) + slot.shape).reshape(zl_size * groups, ROUNDS * SB, shot_dev)
    got = lax.all_to_all(both, ("zl",) + SHOT, 0, 0, tiled=True)
    got = jnp.sum(got.reshape(zl_size, groups, ROUNDS * SB, shot_dev), axis=0)
    mine = jnp.transpose(got, (1, 0, 2)).reshape(1, ROUNDS * SB, groups * shot_dev)
    return mine, receivers


def exchange(part):
    return lax.all_to_all(part, SHOT, 0, 2, tiled=True)


def body(spectra, source_block, taper_window):
    freqs_all, comps, shot_dev, node_dev = spectra.shape
    groups = lax.axis_size("zh") * lax.axis_size("c")
    split = spectra.reshape(groups, 2, freqs_all // (groups * 2), comps, shot_dev, node_dev)
    first = exchange(split[:, 0].reshape(-1, comps, shot_dev, node_dev))
    mine, first = gather_sources(spectra, source_block, first)
    second_part, mine = lax.optimization_barrier((split[:, 1].reshape(-1, comps, shot_dev, node_dev), mine))
    gathered = lax.all_gather(mine, PLANE, axis=0, tiled=True)
    second = exchange(second_part)
    receivers = jnp.concatenate((first, second), axis=0)
    freqs, _, shots, _ = receivers.shape
    source = gathered.reshape(freqs, comps, ROUNDS * SB, shots)
    scale = 1.0 / jnp.sqrt(jnp.float32(shots))
    weight_rows = jnp.repeat(taper_weights(taper_window), SB, axis=0)

    tapered = (source.astype(jnp.float32) * weight_rows[None, None]).astype(jnp.bfloat16)
    real_part = tapered[:, 0]
    imag_part = tapered[:, 1]
    real_row = jnp.concatenate((real_part, imag_part), axis=2)
    imag_row = jnp.concatenate((-imag_part, real_part), axis=2)
    operator = jnp.stack((real_row, imag_row), axis=1)
    stacked = receivers.reshape(freqs, 2 * shots, node_dev)
    summed = jnp.einsum("foqK,fKn->foqn", operator, stacked, preferred_element_type=jnp.float32)
    out = (summed * scale).astype(jnp.bfloat16).reshape(freqs, 2, ROUNDS, SB, node_dev)
    return jnp.transpose(out, (2, 0, 1, 3, 4))


def solution(mesh):
    devices = np.asarray(mesh.devices).reshape(4, 4, 2, 4, 2)
    fine = Mesh(devices, ("y", "x", "zl", "zh", "c"))
    in_specs = (P(None, None, SHOT, ("y", "x", "zl")), P(), P())
    out_specs = P(None, SHOT, None, None, ("y", "x", "zl"))
    return jax.shard_map(body, mesh=fine, in_specs=in_specs, out_specs=out_specs, check_vma=False)
```

```python
import jax
import jax.numpy as jnp
import numpy as np
from jax import lax
from jax.sharding import Mesh, PartitionSpec as P

SB = 32
ROUNDS = 6
WINDOWS = 8
PLANE = ("y", "x")
SHOT = ("zh", "c")


def taper_weights(taper_windows):
    return 0.5 - 0.5 * jnp.cos(jnp.pi * (taper_windows.astype(jnp.float32) + 1.0) / (WINDOWS + 1.0))


def gather_sources(spectra, source_block, receivers=None):
    freqs, comps, shot_dev, node_dev = spectra.shape
    groups = lax.axis_size("zh") * lax.axis_size("c")
    planes = lax.axis_size("y") * lax.axis_size("x")
    zl_size = lax.axis_size("zl")
    per_device = node_dev // SB
    me = (lax.axis_index("y") * lax.axis_size("x") + lax.axis_index("x")) * zl_size + lax.axis_index("zl")
    block = jnp.broadcast_to(source_block[:, None], (ROUNDS, SB)).reshape(ROUNDS * SB)
    column = jnp.arange(ROUNDS * SB, dtype=jnp.int32)
    wanted = block % per_device * SB + column % SB
    keep = block // per_device == me
    node = jnp.arange(node_dev, dtype=jnp.int32)
    select = ((node[:, None] == wanted[None, :]) & keep[None, :]).astype(spectra.dtype)
    by_slot = jnp.transpose(spectra.reshape(groups, planes, shot_dev, node_dev), (1, 0, 2, 3))
    picked = jnp.einsum("pgkn,nq->pgqk", by_slot, select, preferred_element_type=jnp.float32)
    picked = picked.astype(spectra.dtype).reshape(planes * groups, ROUNDS * SB, shot_dev)
    slot = lax.psum_scatter(picked, PLANE, scatter_dimension=0, tiled=True)
    if receivers is not None:
        slot, receivers = lax.optimization_barrier((slot, receivers))
    both = jnp.broadcast_to(slot[None], (zl_size,) + slot.shape).reshape(zl_size * groups, ROUNDS * SB, shot_dev)
    got = lax.all_to_all(both, ("zl",) + SHOT, 0, 0, tiled=True)
    got = jnp.sum(got.reshape(zl_size, groups, ROUNDS * SB, shot_dev), axis=0)
    mine = jnp.transpose(got, (1, 0, 2)).reshape(1, ROUNDS * SB, groups * shot_dev)
    return mine, receivers


def exchange(part):
    return lax.all_to_all(part, SHOT, 0, 2, tiled=True)


def body(spectra, source_block, taper_window):
    freqs_all, comps, shot_dev, node_dev = spectra.shape
    groups = lax.axis_size("zh") * lax.axis_size("c")
    split = spectra.reshape(groups, 2, freqs_all // (groups * 2), comps, shot_dev, node_dev)
    first = exchange(split[:, 0].reshape(-1, comps, shot_dev, node_dev))
    mine, first = gather_sources(spectra, source_block, first)
    second_part, mine = lax.optimization_barrier((split[:, 1].reshape(-1, comps, shot_dev, node_dev), mine))
    gathered = lax.all_gather(mine, PLANE, axis=0, tiled=True)
    second = exchange(second_part)
    receivers = jnp.concatenate((first, second), axis=0)
    freqs, _, shots, _ = receivers.shape
    source = gathered.reshape(freqs, comps, ROUNDS * SB, shots)
    scale = 1.0 / jnp.sqrt(jnp.float32(shots))
    weight_rows = jnp.repeat(taper_weights(taper_window), SB, axis=0)

    tapered = (source.astype(jnp.float32) * weight_rows[None, None]).astype(jnp.bfloat16)
    swapped = jnp.stack((receivers[:, 1], -receivers[:, 0]), axis=1)
    real = jnp.einsum("fcqk,fckn->fqn", tapered, receivers, preferred_element_type=jnp.float32)
    imag = jnp.einsum("fcqk,fckn->fqn", tapered, swapped, preferred_element_type=jnp.float32)
    summed = jnp.stack((real, imag), axis=1)
    out = (summed * scale).astype(jnp.bfloat16).reshape(freqs, 2, ROUNDS, SB, node_dev)
    return jnp.transpose(out, (2, 0, 1, 3, 4))


def solution(mesh):
    devices = np.asarray(mesh.devices).reshape(4, 4, 2, 4, 2)
    fine = Mesh(devices, ("y", "x", "zl", "zh", "c"))
    in_specs = (P(None, None, SHOT, ("y", "x", "zl")), P(), P())
    out_specs = P(None, SHOT, None, None, ("y", "x", "zl"))
    return jax.shard_map(body, mesh=fine, in_specs=in_specs, out_specs=out_specs, check_vma=False)
```

```python
import jax
import jax.numpy as jnp
import numpy as np
from jax import lax
from jax.sharding import Mesh, PartitionSpec as P

SB = 32
ROUNDS = 6
WINDOWS = 8
PLANE = ("y", "x")
SHOT = ("zh", "c")


def taper_weights(taper_windows):
    return 0.5 - 0.5 * jnp.cos(jnp.pi * (taper_windows.astype(jnp.float32) + 1.0) / (WINDOWS + 1.0))


def gather_sources(spectra, source_block, receivers=None):
    freqs, comps, shot_dev, node_dev = spectra.shape
    groups = lax.axis_size("zh") * lax.axis_size("c")
    planes = lax.axis_size("y") * lax.axis_size("x")
    zl_size = lax.axis_size("zl")
    per_device = node_dev // SB
    me = (lax.axis_index("y") * lax.axis_size("x") + lax.axis_index("x")) * zl_size + lax.axis_index("zl")
    block = jnp.broadcast_to(source_block[:, None], (ROUNDS, SB)).reshape(ROUNDS * SB)
    column = jnp.arange(ROUNDS * SB, dtype=jnp.int32)
    wanted = block % per_device * SB + column % SB
    keep = block // per_device == me
    node = jnp.arange(node_dev, dtype=jnp.int32)
    select = ((node[:, None] == wanted[None, :]) & keep[None, :]).astype(spectra.dtype)
    by_slot = jnp.transpose(spectra.reshape(groups, planes, shot_dev, node_dev), (1, 0, 2, 3))
    picked = jnp.einsum("pgkn,nq->pgqk", by_slot, select, preferred_element_type=jnp.float32)
    picked = picked.astype(spectra.dtype).reshape(planes * groups, ROUNDS * SB, shot_dev)
    slot = lax.psum_scatter(picked, PLANE, scatter_dimension=0, tiled=True)
    if receivers is not None:
        slot, receivers = lax.optimization_barrier((slot, receivers))
    both = jnp.broadcast_to(slot[None], (zl_size,) + slot.shape).reshape(zl_size * groups, ROUNDS * SB, shot_dev)
    got = lax.all_to_all(both, ("zl",) + SHOT, 0, 0, tiled=True)
    got = jnp.sum(got.reshape(zl_size, groups, ROUNDS * SB, shot_dev), axis=0)
    mine = jnp.transpose(got, (1, 0, 2)).reshape(1, ROUNDS * SB, groups * shot_dev)
    return mine, receivers


def exchange(part):
    return lax.all_to_all(part, SHOT, 0, 2, tiled=True)


def body(spectra, source_block, taper_window):
    freqs_all, comps, shot_dev, node_dev = spectra.shape
    groups = lax.axis_size("zh") * lax.axis_size("c")
    split = spectra.reshape(groups, 2, freqs_all // (groups * 2), comps, shot_dev, node_dev)
    first = exchange(split[:, 0].reshape(-1, comps, shot_dev, node_dev))
    mine, first = gather_sources(spectra, source_block, first)
    weight_rows = jnp.repeat(taper_weights(taper_window), SB, axis=0)
    mine = (mine.astype(jnp.float32) * weight_rows[None]).astype(jnp.bfloat16)
    second_part, mine = lax.optimization_barrier((split[:, 1].reshape(-1, comps, shot_dev, node_dev), mine))
    gathered = lax.all_gather(mine, PLANE, axis=0, tiled=True)
    second = exchange(second_part)
    receivers = jnp.concatenate((first, second), axis=0)
    freqs, _, shots, _ = receivers.shape
    tapered = gathered.reshape(freqs, comps, ROUNDS * SB, shots)
    scale = 1.0 / jnp.sqrt(jnp.float32(shots))
    swapped = jnp.stack((receivers[:, 1], -receivers[:, 0]), axis=1)
    real = jnp.einsum("fcqk,fckn->fqn", tapered, receivers, preferred_element_type=jnp.float32)
    imag = jnp.einsum("fcqk,fckn->fqn", tapered, swapped, preferred_element_type=jnp.float32)
    summed = jnp.stack((real, imag), axis=1)
    out = (summed * scale).astype(jnp.bfloat16).reshape(freqs, 2, ROUNDS, SB, node_dev)
    return jnp.transpose(out, (2, 0, 1, 3, 4))


def solution(mesh):
    devices = np.asarray(mesh.devices).reshape(4, 4, 2, 4, 2)
    fine = Mesh(devices, ("y", "x", "zl", "zh", "c"))
    in_specs = (P(None, None, SHOT, ("y", "x", "zl")), P(), P())
    out_specs = P(None, SHOT, None, None, ("y", "x", "zl"))
    return jax.shard_map(body, mesh=fine, in_specs=in_specs, out_specs=out_specs, check_vma=False)
```
